256 devices in a mesh: group: 8 (over x, core), inner: 32 (over z, y).
Axes of the slice: x: 4, y: 4, z: 8, core: 2. Of those that a mesh axis runs over, the one named last changes fastest.
Arguments:
- flow_field: float32 [1536, 1536, 128], P('inner', 'group'), may hold values from -6 to 6
- sketch_rows: float32 [1536, 128], P('inner'), may hold values from -6 to 6
- sketch_cols: float32 [1536, 128], P('group'), may hold values from -6 to 6
- sketch_depth: float32 [128, 128], replicated, may hold values from -6 to 6
- bit_widths: int32 [2], replicated, may hold values from 6 to 8
- bin_edges: int32 [9], replicated, may hold values from -6 to 6, as said below
Outputs:
- basis_one: float32 [1536, 128], P('inner')
- basis_two: float32 [1536, 128], P('group')
- core: float32 [128, 128, 128], P('inner', 'group')
- residual: float32 [2, 128, 128, 128], P(None, 'inner', 'group')
- energy: float32 [2, 1536, 128], P(None, 'inner')
- histogram: float32 [2, 1536, 8], P(None, 'inner')
The draws below stay inside these ranges and needn't reach their ends.
Inputs may be any that keep to these rules, and one draw needn't show every extreme that they name: `bin_edges`: strictly increasing; the first is -6 and the last 6.
All inputs are finite; a program needn't handle non-finite values.
Results may differ from the reference program's by a relative error of at most 0.0008.
Values sent between devices are 32-bit elements; how exact they have to be, the bound alone decides.
No kernel may reach another device: no remote copies, remote signals or barrier semaphores. Data moves between devices by JAX's collectives and lax.ppermute only.
A program may use at most 128 MiB of HBM per device.

```python
import jax
import jax.numpy as jnp
from jax import lax

N1 = 1536
N2 = 1536
N3 = 128
R = 128
NB = 2
NEDGE = 9
EDGE_SPAN = 6
NBINS = 8


def draw_bin_edges(key, part):
    candidates = jax.random.permutation(key, 2 * EDGE_SPAN - 1)[:NEDGE - 2]
    middle_edges = jnp.sort(candidates).astype(jnp.int32) - (EDGE_SPAN - 1)
    low_end = jnp.full((1,), -EDGE_SPAN, jnp.int32)
    high_end = jnp.full((1,), EDGE_SPAN, jnp.int32)
    return jnp.concatenate([low_end, middle_edges, high_end]).astype(jnp.int32)


def level_of(key, dims, split, low, largest):
    level = 1.0
    for axis_at, shards_of in split:
        steps = jax.random.uniform(jax.random.fold_in(jax.random.fold_in(key, 6), axis_at), (shards_of,), jnp.float32, low / len(split), largest / len(split))
        level = level * jnp.repeat(jnp.exp(steps), dims[axis_at] // shards_of).reshape((-1,) + (1,) * (len(dims) - 1 - axis_at))
    return level


def noise(rng, shape, deviation, limit, cuts=(), dtype=jnp.bfloat16):
    drawn = deviation * jax.random.normal(rng, shape, jnp.float32)
    if cuts:
        drawn = drawn * level_of(rng, shape, cuts, -0.22, 0.18)
    return jnp.clip(drawn, -limit, limit).astype(dtype)


def setup_inputs(seed: int = 0) -> dict:
    arg_keys = jax.random.split(jax.random.key(seed), 7)
    return {
        "flow_field": noise(arg_keys[0], (N1, N2, N3), 1.0, 6.0, ((0, 32), (1, 8)), jnp.float32),
        "sketch_rows": noise(arg_keys[1], (N1, R), 1.0, 6.0, ((0, 32),), jnp.float32),
        "sketch_cols": noise(arg_keys[2], (N2, R), 1.0, 6.0, ((0, 8),), jnp.float32),
        "sketch_depth": noise(arg_keys[3], (N3, R), 1.0, 6.0, (), jnp.float32),
        "bit_widths": jax.random.randint(arg_keys[4], (NB,), 6, 9).astype(jnp.int32),
        "bin_edges": draw_bin_edges(jax.random.fold_in(arg_keys[6], 71), 0),
    }


precise = lax.Precision.HIGHEST
two_pi = 2.0 * 3.141592653589793
error_boost = 16.0
row_block = 32

def orthonormal(sketch):
    gram_matrix = jnp.dot(sketch.T, sketch, precision=precise)
    lower_factor = jnp.linalg.cholesky(gram_matrix)
    return jax.scipy.linalg.solve_triangular(lower_factor, sketch.T, lower=True).T

def reference(flow_field, sketch_rows, sketch_cols, sketch_depth, bit_widths, bin_edges):

    def row_step(running, inputs):
        field_row, weight = inputs
        reduced = jnp.dot(field_row, sketch_depth, precision=precise)
        first_mode = jnp.sum(reduced * sketch_cols, axis=0)
        return (running + reduced * weight[None, :], first_mode)
    mode_two, mode_one = lax.scan(row_step, jnp.zeros((N2, R), jnp.float32), (flow_field, sketch_rows))
    basis_one = orthonormal(mode_one)
    basis_two = orthonormal(mode_two)
    along_two = jnp.einsum('ijk,js->isk', flow_field, basis_two, precision=precise)
    core_values = jnp.einsum('ir,isk->rsk', basis_one, along_two, precision=precise)
    peak = jnp.max(jnp.abs(core_values))
    levels = jnp.exp2(bit_widths.astype(jnp.float32) - 1.0) - 1.0
    step_size = peak / levels
    residual = -jnp.sin(two_pi * core_values[None] / step_size[:, None, None, None]) / two_pi
    error_scale = error_boost * (N1 * N2) ** 0.5 / R
    edge_values = bin_edges.astype(jnp.float32)
    blocks = basis_one.reshape(N1 // row_block, row_block, R)

    def block_stats(block_basis):
        mixed_core = jnp.einsum('ir,brsk->bisk', block_basis, residual, precision=precise)
        field_error = error_scale * jnp.einsum('bisk,js->bijk', mixed_core, basis_two, precision=precise)
        energy_part = jnp.sum(field_error * field_error, axis=2) / N2
        ramp_sums = jnp.stack([jnp.sum(jnp.clip(field_error - edge_values[index_edge] + 0.5, 0.0, 1.0), axis=(2, 3)) for index_edge in range(NEDGE)], axis=-1)
        return (energy_part, ramp_sums)
    energy_blocks, ramp_blocks = lax.map(block_stats, blocks)
    energy = jnp.transpose(energy_blocks, (1, 0, 2, 3)).reshape(NB, N1, N3)
    ramp_sums = jnp.transpose(ramp_blocks, (1, 0, 2, 3)).reshape(NB, N1, NEDGE)
    histogram = (ramp_sums[..., :-1] - ramp_sums[..., 1:]) * (NBINS / (N2 * N3))
    return (basis_one, basis_two, core_values, residual, energy, histogram)
```

```python
import math

import jax
import jax.numpy as jnp
from jax import lax
from jax.sharding import PartitionSpec as P

NEDGE = 9
NBINS = 8


precise = lax.Precision.HIGHEST
two_pi = 2.0 * 3.141592653589793
error_boost = 16.0


def gram_of(sketch):
    return jnp.dot(sketch.T, sketch, precision=precise)


def orthonormal_rows(sketch, gram_matrix):
    lower_factor = jnp.linalg.cholesky(gram_matrix)
    return jax.scipy.linalg.solve_triangular(lower_factor, sketch.T, lower=True).T


def soft_residual(core_values, step_size):
    shape = (-1,) + (1,) * core_values.ndim
    return -jnp.sin(two_pi * core_values[None] / step_size.reshape(shape)) / two_pi


def xor_pairs(n, d):
    return [(a, a ^ d) for a in range(n)]


def bits_of(n):
    return [1 << t for t in range(n.bit_length() - 1)]


def all_reduce(x, axis, n, op=jnp.add):
    for d in bits_of(n):
        x = op(x, lax.ppermute(x, axis, xor_pairs(n, d)))
    return x


def reduce_scatter(x, axis, n):
    idx = lax.axis_index(axis)
    nb = n.bit_length() - 1
    chunk = x.shape[0] // n
    rest = x.shape[1:]
    x = x.reshape((2,) * nb + (chunk,) + rest)
    left = list(range(nb))
    for d in bits_of(n):
        t = left.index(nb - 1 - (d.bit_length() - 1))
        bit = (idx // d) % 2
        keep = lax.dynamic_index_in_dim(x, bit, axis=t, keepdims=False)
        send = lax.dynamic_index_in_dim(x, 1 - bit, axis=t, keepdims=False)
        x = keep + lax.ppermute(send, axis, xor_pairs(n, d))
        left.pop(t)
    return x.reshape((chunk,) + rest)


def all_gather(x, axis, n):
    idx = lax.axis_index(axis)
    nb = n.bit_length() - 1
    chunk = x.shape[0]
    rest = x.shape[1:]
    have = []
    for d in reversed(bits_of(n)):
        pos = nb - 1 - (d.bit_length() - 1)
        t = sum(1 for h in have if h < pos)
        other = lax.ppermute(x, axis, xor_pairs(n, d))
        bit = (idx // d) % 2
        x = jnp.where(bit == 0, jnp.stack([x, other], axis=t), jnp.stack([other, x], axis=t))
        have.append(pos)
        have.sort()
    return x.reshape((n * chunk,) + rest)


def make_local(n_group, n_inner):
    def local(flow_field, sketch_rows, sketch_cols, sketch_depth, bit_widths, bin_edges):
        rows_i, cols_j, depth_k = flow_field.shape
        rank = sketch_depth.shape[1]
        n1 = rows_i * n_inner
        n2 = cols_j * n_group
        k_blk = depth_k // n_group
        r_blk = rank // n_inner
        s_blk = rank // n_group
        g = lax.axis_index("group")
        p = lax.axis_index("inner")

        reduced = jnp.einsum("ijk,kr->ijr", flow_field, sketch_depth, precision=precise)
        mode_one = jnp.einsum("ijr,jr->ir", reduced, sketch_cols, precision=precise)
        mode_two = jnp.einsum("ijr,ir->jr", reduced, sketch_rows, precision=precise)
        mode_one = all_reduce(mode_one, "group", n_group)
        mode_two = all_reduce(mode_two, "inner", n_inner)
        basis_one = orthonormal_rows(mode_one, all_reduce(gram_of(mode_one), "inner", n_inner))
        basis_two = orthonormal_rows(mode_two, all_reduce(gram_of(mode_two), "group", n_group))
        basis_two_all = all_gather(basis_two, "group", n_group)

        along_two = jnp.einsum("ijk,js->kis", flow_field, basis_two, precision=precise)
        along_two = reduce_scatter(along_two, "group", n_group)
        partial = jnp.einsum("kis,ir->krs", along_two, basis_one, precision=precise)
        partial = partial.reshape(k_blk * rank, rank)
        core_part = reduce_scatter(partial, "inner", n_inner)
        peak = all_reduce(jnp.max(jnp.abs(core_part)), "inner", n_inner, jnp.maximum)
        peak = all_reduce(peak, "group", n_group, jnp.maximum)
        core_k = all_gather(core_part, "inner", n_inner).reshape(k_blk, rank, rank)

        levels = jnp.exp2(bit_widths.astype(jnp.float32) - 1.0) - 1.0
        step = peak / levels
        residual_k = soft_residual(core_k, step)

        core_rows = lax.dynamic_slice_in_dim(core_k, p * r_blk, r_blk, axis=1)
        core_rows = all_gather(core_rows, "group", n_group)
        core_block = lax.dynamic_slice_in_dim(core_rows, g * s_blk, s_blk, axis=2)
        core_block = jnp.transpose(core_block, (1, 2, 0))
        residual_block = soft_residual(core_block, step)

        mixed = jnp.einsum("ir,bkrs->sbik", basis_one, residual_k, precision=precise)
        nb = mixed.shape[1]
        mixed = mixed.reshape(rank, nb * rows_i * k_blk)
        error_scale = error_boost * math.sqrt(n1 * n2) / rank
        field_error = error_scale * jnp.dot(basis_two_all, mixed, precision=precise)
        energy_part = (jnp.sum(field_error * field_error, axis=0) / n2).reshape(nb, rows_i, k_blk)
        edge_values = bin_edges.astype(jnp.float32)
        ramp_part = jnp.stack(
            [
                jnp.sum(
                    jnp.clip(field_error - edge_values[index_edge] + 0.5, 0.0, 1.0), axis=0
                ).reshape(nb, rows_i, k_blk).sum(axis=2)
                for index_edge in range(NEDGE)
            ],
            axis=-1,
        )
        energy_slot = jnp.zeros((nb, rows_i, depth_k), jnp.float32)
        energy_slot = lax.dynamic_update_slice_in_dim(energy_slot, energy_part, g * k_blk, axis=2)
        packed = all_reduce(jnp.concatenate([energy_slot, ramp_part], axis=2), "group", n_group)
        energy = packed[:, :, :depth_k]
        ramp_sums = packed[:, :, depth_k:]
        histogram = (ramp_sums[..., :-1] - ramp_sums[..., 1:]) * (NBINS / (n2 * depth_k))
        return (basis_one, basis_two, core_block, residual_block, energy, histogram)

    return local


def solution(mesh):
    in_specs = (P("inner", "group", None), P("inner", None), P("group", None), P(), P(), P())
    out_specs = (
        P("inner", None),
        P("group", None),
        P("inner", "group", None),
        P(None, "inner", "group", None),
        P(None, "inner", None),
        P(None, "inner", None),
    )
    local = make_local(mesh.shape["group"], mesh.shape["inner"])
    return jax.shard_map(local, mesh=mesh, in_specs=in_specs, out_specs=out_specs, check_vma=False)
```

```python
import math

import jax
import jax.numpy as jnp
from jax import lax
from jax.sharding import PartitionSpec as P

NEDGE = 9
NBINS = 8


precise = lax.Precision.HIGHEST
two_pi = 2.0 * 3.141592653589793
error_boost = 16.0


def gram_of(sketch):
    return jnp.dot(sketch.T, sketch, precision=precise)


def orthonormal_rows(sketch, gram_matrix):
    lower_factor = jnp.linalg.cholesky(gram_matrix)
    return jax.scipy.linalg.solve_triangular(lower_factor, sketch.T, lower=True).T


def soft_residual(core_values, step_size):
    shape = (-1,) + (1,) * core_values.ndim
    return -jnp.sin(two_pi * core_values[None] / step_size.reshape(shape)) / two_pi


def xor_pairs(n, d):
    return [(a, a ^ d) for a in range(n)]


def bits_of(n):
    return [1 << t for t in range(n.bit_length() - 1)]


def all_reduce(x, axis, n, op=jnp.add):
    for d in bits_of(n):
        x = op(x, lax.ppermute(x, axis, xor_pairs(n, d)))
    return x


def reduce_scatter(x, axis, n):
    idx = lax.axis_index(axis)
    nb = n.bit_length() - 1
    chunk = x.shape[0] // n
    rest = x.shape[1:]
    x = x.reshape((2,) * nb + (chunk,) + rest)
    left = list(range(nb))
    for d in bits_of(n):
        t = left.index(nb - 1 - (d.bit_length() - 1))
        bit = (idx // d) % 2
        keep = lax.dynamic_index_in_dim(x, bit, axis=t, keepdims=False)
        send = lax.dynamic_index_in_dim(x, 1 - bit, axis=t, keepdims=False)
        x = keep + lax.ppermute(send, axis, xor_pairs(n, d))
        left.pop(t)
    return x.reshape((chunk,) + rest)


def all_gather(x, axis, n, flat=True):
    idx = lax.axis_index(axis)
    nb = n.bit_length() - 1
    have = []
    for d in reversed(bits_of(n)):
        pos = nb - 1 - (d.bit_length() - 1)
        t = sum(1 for h in have if h < pos)
        other = lax.ppermute(x, axis, xor_pairs(n, d))
        bit = (idx // d) % 2
        x = jnp.where(bit == 0, jnp.stack([x, other], axis=t), jnp.stack([other, x], axis=t))
        have.append(pos)
        have.sort()
    x = x.reshape((n,) + x.shape[nb:])
    if flat:
        x = x.reshape((-1,) + x.shape[2:])
    return x


def make_local(n_group, n_inner):
    def local(flow_field, sketch_rows, sketch_cols, sketch_depth, bit_widths, bin_edges):
        rows_i, cols_j, depth_k = flow_field.shape
        rank = sketch_depth.shape[1]
        n1 = rows_i * n_inner
        n2 = cols_j * n_group
        k_blk = depth_k // n_group
        r_blk = rank // n_inner
        s_blk = rank // n_group
        g = lax.axis_index("group")
        p = lax.axis_index("inner")

        reduced = jnp.einsum("ijk,kr->ijr", flow_field, sketch_depth, precision=precise)
        mode_one = jnp.einsum("ijr,jr->ir", reduced, sketch_cols, precision=precise)
        mode_two = jnp.einsum("ijr,ir->jr", reduced, sketch_rows, precision=precise)
        mode_one = all_reduce(mode_one, "group", n_group)
        packed = all_reduce(
            jnp.concatenate([gram_of(mode_one), mode_two], axis=0), "inner", n_inner
        )
        gram_one = packed[:rank]
        mode_two = packed[rank:]
        basis_two = orthonormal_rows(mode_two, all_reduce(gram_of(mode_two), "group", n_group))
        basis_one = orthonormal_rows(mode_one, gram_one)
        basis_two_all = all_gather(basis_two, "group", n_group)

        along_two = jnp.einsum("ijk,js->kis", flow_field, basis_two, precision=precise)
        along_two = reduce_scatter(along_two, "group", n_group)
        partial = jnp.einsum("kis,ir->krs", along_two, basis_one, precision=precise)
        partial = partial.reshape(k_blk * rank, rank)
        core_part = reduce_scatter(partial, "inner", n_inner)
        mark = jnp.broadcast_to(jnp.max(jnp.abs(core_part)), (8, rank))
        gathered = all_gather(jnp.concatenate([core_part, mark], axis=0), "inner", n_inner, flat=False)
        core_k = gathered[:, : core_part.shape[0]].reshape(k_blk, rank, rank)
        peak = jnp.max(gathered[:, core_part.shape[0]:])

        core_rows = lax.dynamic_slice_in_dim(core_k, p * r_blk, r_blk, axis=1)
        mark = jnp.broadcast_to(peak, (1, r_blk, rank))
        gathered = all_gather(jnp.concatenate([core_rows, mark], axis=0), "group", n_group, flat=False)
        core_rows = gathered[:, :k_blk].reshape(depth_k, r_blk, rank)
        peak = jnp.max(gathered[:, k_blk:])
        core_block = lax.dynamic_slice_in_dim(core_rows, g * s_blk, s_blk, axis=2)
        core_block = jnp.transpose(core_block, (1, 2, 0))

        levels = jnp.exp2(bit_widths.astype(jnp.float32) - 1.0) - 1.0
        step = peak / levels
        residual_k = soft_residual(core_k, step)
        residual_block = soft_residual(core_block, step)

        mixed = jnp.einsum("ir,bkrs->sbik", basis_one, residual_k, precision=precise)
        nb = mixed.shape[1]
        mixed = mixed.reshape(rank, nb * rows_i * k_blk)
        error_scale = error_boost * math.sqrt(n1 * n2) / rank
        field_error = error_scale * jnp.dot(basis_two_all, mixed, precision=precise)
        energy_part = (jnp.sum(field_error * field_error, axis=0) / n2).reshape(nb, rows_i, k_blk)
        edge_values = bin_edges.astype(jnp.float32)
        ramp_part = jnp.stack(
            [
                jnp.sum(
                    jnp.clip(field_error - edge_values[index_edge] + 0.5, 0.0, 1.0), axis=0
                ).reshape(nb, rows_i, k_blk).sum(axis=2)
                for index_edge in range(NEDGE)
            ],
            axis=-1,
        )
        energy_slot = jnp.zeros((nb, rows_i, depth_k), jnp.float32)
        energy_slot = lax.dynamic_update_slice_in_dim(energy_slot, energy_part, g * k_blk, axis=2)
        packed = all_reduce(jnp.concatenate([energy_slot, ramp_part], axis=2), "group", n_group)
        energy = packed[:, :, :depth_k]
        ramp_sums = packed[:, :, depth_k:]
        histogram = (ramp_sums[..., :-1] - ramp_sums[..., 1:]) * (NBINS / (n2 * depth_k))
        return (basis_one, basis_two, core_block, residual_block, energy, histogram)

    return local


def solution(mesh):
    in_specs = (P("inner", "group", None), P("inner", None), P("group", None), P(), P(), P())
    out_specs = (
        P("inner", None),
        P("group", None),
        P("inner", "group", None),
        P(None, "inner", "group", None),
        P(None, "inner", None),
        P(None, "inner", None),
    )
    local = make_local(mesh.shape["group"], mesh.shape["inner"])
    return jax.shard_map(local, mesh=mesh, in_specs=in_specs, out_specs=out_specs, check_vma=False)
```

```python
import math

import jax
import jax.numpy as jnp
from jax import lax
from jax.sharding import PartitionSpec as P

NEDGE = 9
NBINS = 8


precise = lax.Precision.HIGHEST
two_pi = 2.0 * 3.141592653589793
error_boost = 16.0


def gram_of(sketch):
    return jnp.dot(sketch.T, sketch, precision=precise)


def orthonormal_rows(sketch, gram_matrix):
    lower_factor = jnp.linalg.cholesky(gram_matrix)
    return jax.scipy.linalg.solve_triangular(lower_factor, sketch.T, lower=True).T


def soft_residual(core_values, step_size):
    shape = (-1,) + (1,) * core_values.ndim
    return -jnp.sin(two_pi * core_values[None] / step_size.reshape(shape)) / two_pi


def xor_pairs(n, d):
    return [(a, a ^ d) for a in range(n)]


def bits_of(n):
    return [1 << t for t in range(n.bit_length() - 1)]


def all_reduce(x, axis, n, op=jnp.add):
    for d in bits_of(n):
        x = op(x, lax.ppermute(x, axis, xor_pairs(n, d)))
    return x


def reduce_scatter(x, axis, n):
    idx = lax.axis_index(axis)
    nb = n.bit_length() - 1
    chunk = x.shape[0] // n
    rest = x.shape[1:]
    x = x.reshape((2,) * nb + (chunk,) + rest)
    left = list(range(nb))
    for d in bits_of(n):
        t = left.index(nb - 1 - (d.bit_length() - 1))
        bit = (idx // d) % 2
        keep = lax.dynamic_index_in_dim(x, bit, axis=t, keepdims=False)
        send = lax.dynamic_index_in_dim(x, 1 - bit, axis=t, keepdims=False)
        x = keep + lax.ppermute(send, axis, xor_pairs(n, d))
        left.pop(t)
    return x.reshape((chunk,) + rest)


def all_gather(x, axis, n, flat=True):
    idx = lax.axis_index(axis)
    nb = n.bit_length() - 1
    have = []
    for d in reversed(bits_of(n)):
        pos = nb - 1 - (d.bit_length() - 1)
        t = sum(1 for h in have if h < pos)
        other = lax.ppermute(x, axis, xor_pairs(n, d))
        bit = (idx // d) % 2
        x = jnp.where(bit == 0, jnp.stack([x, other], axis=t), jnp.stack([other, x], axis=t))
        have.append(pos)
        have.sort()
    x = x.reshape((n,) + x.shape[nb:])
    if flat:
        x = x.reshape((-1,) + x.shape[2:])
    return x


def make_local(n_group, n_inner):
    def local(flow_field, sketch_rows, sketch_cols, sketch_depth, bit_widths, bin_edges):
        rows_i, cols_j, depth_k = flow_field.shape
        rank = sketch_depth.shape[1]
        n1 = rows_i * n_inner
        n2 = cols_j * n_group
        k_blk = depth_k // n_group
        r_blk = rank // n_inner
        s_blk = rank // n_group
        g = lax.axis_index("group")
        p = lax.axis_index("inner")

        reduced = jnp.einsum("ijk,kr->ijr", flow_field, sketch_depth, precision=precise)
        mode_one = jnp.einsum("ijr,jr->ir", reduced, sketch_cols, precision=precise)
        mode_two = jnp.einsum("ijr,ir->jr", reduced, sketch_rows, precision=precise)
        mode_one = all_reduce(mode_one, "group", n_group)
        packed = all_reduce(
            jnp.concatenate([gram_of(mode_one), mode_two], axis=0), "inner", n_inner
        )
        gram_one = packed[:rank]
        mode_two = packed[rank:]
        basis_two = orthonormal_rows(mode_two, all_reduce(gram_of(mode_two), "group", n_group))
        basis_one = orthonormal_rows(mode_one, gram_one)
        basis_two_all = all_gather(basis_two, "group", n_group)

        along_two = jnp.einsum("ijk,js->kis", flow_field, basis_two, precision=precise)
        along_two = reduce_scatter(along_two, "group", n_group)
        partial = jnp.einsum("kis,ir->krs", along_two, basis_one, precision=precise)
        partial = partial.reshape(k_blk * rank, rank)
        core_part = reduce_scatter(partial, "inner", n_inner)
        mark = jnp.broadcast_to(jnp.max(jnp.abs(core_part)), (8, rank))
        gathered = all_gather(jnp.concatenate([core_part, mark], axis=0), "inner", n_inner, flat=False)
        core_k = gathered[:, : core_part.shape[0]].reshape(k_blk, rank, rank)
        peak = jnp.max(gathered[:, core_part.shape[0]:])

        core_rows = lax.dynamic_slice_in_dim(core_k, p * r_blk, r_blk, axis=1)
        mark = jnp.broadcast_to(peak, (1, r_blk, rank))
        gathered = all_gather(jnp.concatenate([core_rows, mark], axis=0), "group", n_group, flat=False)
        core_rows = gathered[:, :k_blk].reshape(depth_k, r_blk, rank)
        peak = jnp.max(gathered[:, k_blk:])
        core_block = lax.dynamic_slice_in_dim(core_rows, g * s_blk, s_blk, axis=2)
        core_block = jnp.transpose(core_block, (1, 2, 0))

        levels = jnp.exp2(bit_widths.astype(jnp.float32) - 1.0) - 1.0
        step = peak / levels
        residual_k = soft_residual(core_k, step)
        residual_block = soft_residual(core_block, step)

        error_scale = error_boost * math.sqrt(n1 * n2) / rank
        edge_values = bin_edges.astype(jnp.float32)
        nb = residual_k.shape[0]
        sums = []
        for b in range(nb):
            mixed = jnp.einsum("ir,krs->sik", basis_one, residual_k[b], precision=lax.Precision.HIGH)
            mixed = mixed.reshape(rank, rows_i * k_blk)
            field_error = error_scale * jnp.dot(basis_two_all, mixed, precision=lax.Precision.HIGH)
            energy_part = (jnp.sum(field_error * field_error, axis=0) / n2).reshape(rows_i, k_blk)
            shifted = field_error + 0.5
            ramp_part = jnp.stack(
                [
                    (
                        jnp.sum(
                            jnp.clip(shifted, edge_values[index_edge], edge_values[index_edge] + 1.0),
                            axis=0,
                        )
                        - field_error.shape[0] * edge_values[index_edge]
                    ).reshape(rows_i, k_blk).sum(axis=1)
                    for index_edge in range(NEDGE)
                ],
                axis=-1,
            )
            energy_slot = jnp.zeros((rows_i, depth_k), jnp.float32)
            energy_slot = lax.dynamic_update_slice_in_dim(energy_slot, energy_part, g * k_blk, axis=1)
            sums.append(all_reduce(jnp.concatenate([energy_slot, ramp_part], axis=1), "group", n_group))
        packed = jnp.stack(sums)
        energy = packed[:, :, :depth_k]
        ramp_sums = packed[:, :, depth_k:]
        histogram = (ramp_sums[..., :-1] - ramp_sums[..., 1:]) * (NBINS / (n2 * depth_k))
        return (basis_one, basis_two, core_block, residual_block, energy, histogram)

    return local


def solution(mesh):
    in_specs = (P("inner", "group", None), P("inner", None), P("group", None), P(), P(), P())
    out_specs = (
        P("inner", None),
        P("group", None),
        P("inner", "group", None),
        P(None, "inner", "group", None),
        P(None, "inner", None),
        P(None, "inner", None),
    )
    local = make_local(mesh.shape["group"], mesh.shape["inner"])
    return jax.shard_map(local, mesh=mesh, in_specs=in_specs, out_specs=out_specs, check_vma=False)
```

```python
import math

import jax
import jax.numpy as jnp
from jax import lax
from jax.sharding import PartitionSpec as P

NEDGE = 9
NBINS = 8


precise = lax.Precision.HIGHEST
two_pi = 2.0 * 3.141592653589793
error_boost = 16.0


def gram_of(sketch):
    return jnp.dot(sketch.T, sketch, precision=precise)


def orthonormal_rows(sketch, gram_matrix):
    lower_factor = jnp.linalg.cholesky(gram_matrix)
    return jax.scipy.linalg.solve_triangular(lower_factor, sketch.T, lower=True).T


def soft_residual(core_values, step_size):
    shape = (-1,) + (1,) * core_values.ndim
    return -jnp.sin(two_pi * core_values[None] / step_size.reshape(shape)) / two_pi


def xor_pairs(n, d):
    return [(a, a ^ d) for a in range(n)]


def bits_of(n):
    return [1 << t for t in range(n.bit_length() - 1)]


def all_reduce(x, axis, n, op=jnp.add):
    for d in bits_of(n):
        x = op(x, lax.ppermute(x, axis, xor_pairs(n, d)))
    return x


def reduce_scatter(x, axis, n):
    idx = lax.axis_index(axis)
    nb = n.bit_length() - 1
    chunk = x.shape[0] // n
    rest = x.shape[1:]
    x = x.reshape((2,) * nb + (chunk,) + rest)
    left = list(range(nb))
    for d in bits_of(n):
        t = left.index(nb - 1 - (d.bit_length() - 1))
        bit = (idx // d) % 2
        keep = lax.dynamic_index_in_dim(x, bit, axis=t, keepdims=False)
        send = lax.dynamic_index_in_dim(x, 1 - bit, axis=t, keepdims=False)
        x = keep + lax.ppermute(send, axis, xor_pairs(n, d))
        left.pop(t)
    return x.reshape((chunk,) + rest)


def all_gather(x, axis, n, flat=True):
    idx = lax.axis_index(axis)
    nb = n.bit_length() - 1
    have = []
    for d in reversed(bits_of(n)):
        pos = nb - 1 - (d.bit_length() - 1)
        t = sum(1 for h in have if h < pos)
        other = lax.ppermute(x, axis, xor_pairs(n, d))
        bit = (idx // d) % 2
        x = jnp.where(bit == 0, jnp.stack([x, other], axis=t), jnp.stack([other, x], axis=t))
        have.append(pos)
        have.sort()
    x = x.reshape((n,) + x.shape[nb:])
    if flat:
        x = x.reshape((-1,) + x.shape[2:])
    return x


def make_local(n_group, n_inner):
    def local(flow_field, sketch_rows, sketch_cols, sketch_depth, bit_widths, bin_edges):
        rows_i, cols_j, depth_k = flow_field.shape
        rank = sketch_depth.shape[1]
        n1 = rows_i * n_inner
        n2 = cols_j * n_group
        k_blk = depth_k // n_group
        r_blk = rank // n_inner
        s_blk = rank // n_group
        g = lax.axis_index("group")
        p = lax.axis_index("inner")

        reduced = jnp.einsum("ijk,kr->ijr", flow_field, sketch_depth, precision=precise)
        mode_one = jnp.einsum("ijr,jr->ir", reduced, sketch_cols, precision=precise)
        mode_two = jnp.einsum("ijr,ir->jr", reduced, sketch_rows, precision=precise)
        mode_two = all_reduce(mode_two, "inner", n_inner)
        packed = all_reduce(jnp.concatenate([gram_of(mode_two), mode_one], axis=0), "group", n_group)
        basis_two = orthonormal_rows(mode_two, packed[:rank])
        mode_one = packed[rank:]
        lower_one = jnp.linalg.cholesky(all_reduce(gram_of(mode_one), "inner", n_inner))
        basis_one = jax.scipy.linalg.solve_triangular(lower_one, mode_one.T, lower=True).T
        inverse_one = jax.scipy.linalg.solve_triangular(
            lower_one, jnp.eye(rank, dtype=jnp.float32), lower=True
        )
        basis_two_all = all_gather(basis_two, "group", n_group)

        along_two = jnp.einsum("ijk,js->kis", flow_field, basis_two, precision=precise)
        along_two = reduce_scatter(along_two, "group", n_group)
        partial = jnp.einsum("kis,ir->krs", along_two, mode_one, precision=precise)
        partial = partial.reshape(k_blk * rank, rank)
        core_part = reduce_scatter(partial, "inner", n_inner)
        raw_k = all_gather(core_part, "inner", n_inner).reshape(k_blk, rank, rank)
        core_k = jnp.einsum("qr,krs->kqs", inverse_one, raw_k, precision=precise)
        peak = jnp.max(jnp.abs(core_k))

        core_rows = lax.dynamic_slice_in_dim(core_k, p * r_blk, r_blk, axis=1)
        mark = jnp.broadcast_to(peak, (1, r_blk, rank))
        gathered = all_gather(jnp.concatenate([core_rows, mark], axis=0), "group", n_group, flat=False)
        core_rows = gathered[:, :k_blk].reshape(depth_k, r_blk, rank)
        peak = jnp.max(gathered[:, k_blk:])
        core_block = lax.dynamic_slice_in_dim(core_rows, g * s_blk, s_blk, axis=2)
        core_block = jnp.transpose(core_block, (1, 2, 0))

        levels = jnp.exp2(bit_widths.astype(jnp.float32) - 1.0) - 1.0
        step = peak / levels
        residual_k = soft_residual(core_k, step)
        residual_block = soft_residual(core_block, step)

        error_scale = error_boost * math.sqrt(n1 * n2) / rank
        edge_values = bin_edges.astype(jnp.float32)
        mixed = jnp.einsum("ir,bkrs->sbik", basis_one, residual_k, precision=lax.Precision.HIGH)
        nb = mixed.shape[1]
        mixed = mixed.reshape(rank, nb * rows_i * k_blk)
        field_error = error_scale * jnp.dot(basis_two_all, mixed, precision=lax.Precision.HIGH)
        energy_part = (jnp.sum(field_error * field_error, axis=0) / n2).reshape(nb, rows_i, k_blk)
        shifted = field_error + 0.5
        ramp_part = jnp.stack(
            [
                (
                    jnp.sum(
                        jnp.clip(shifted, edge_values[index_edge], edge_values[index_edge] + 1.0),
                        axis=0,
                    )
                    - field_error.shape[0] * edge_values[index_edge]
                ).reshape(nb, rows_i, k_blk).sum(axis=2)
                for index_edge in range(NEDGE)
            ],
            axis=-1,
        )
        energy_slot = jnp.zeros((nb, rows_i, depth_k), jnp.float32)
        energy_slot = lax.dynamic_update_slice_in_dim(energy_slot, energy_part, g * k_blk, axis=2)
        packed = all_reduce(jnp.concatenate([energy_slot, ramp_part], axis=2), "group", n_group)
        energy = packed[:, :, :depth_k]
        ramp_sums = packed[:, :, depth_k:]
        histogram = (ramp_sums[..., :-1] - ramp_sums[..., 1:]) * (NBINS / (n2 * depth_k))
        return (basis_one, basis_two, core_block, residual_block, energy, histogram)

    return local


def solution(mesh):
    in_specs = (P("inner", "group", None), P("inner", None), P("group", None), P(), P(), P())
    out_specs = (
        P("inner", None),
        P("group", None),
        P("inner", "group", None),
        P(None, "inner", "group", None),
        P(None, "inner", None),
        P(None, "inner", None),
    )
    local = make_local(mesh.shape["group"], mesh.shape["inner"])
    return jax.shard_map(local, mesh=mesh, in_specs=in_specs, out_specs=out_specs, check_vma=False)
```

```python
import math

import jax
import jax.numpy as jnp
from jax import lax
from jax.sharding import PartitionSpec as P

NEDGE = 9
NBINS = 8


precise = lax.Precision.HIGHEST
two_pi = 2.0 * 3.141592653589793
error_boost = 16.0


def gram_of(sketch):
    return jnp.dot(sketch.T, sketch, precision=precise)


def orthonormal_rows(sketch, gram_matrix):
    lower_factor = jnp.linalg.cholesky(gram_matrix)
    return jax.scipy.linalg.solve_triangular(lower_factor, sketch.T, lower=True).T


def soft_residual(core_values, step_size):
    shape = (-1,) + (1,) * core_values.ndim
    return -jnp.sin(two_pi * core_values[None] / step_size.reshape(shape)) / two_pi


def xor_pairs(n, d):
    return [(a, a ^ d) for a in range(n)]


def bits_of(n):
    return [1 << t for t in range(n.bit_length() - 1)]


def all_reduce(x, axis, n, op=jnp.add):
    for d in bits_of(n):
        x = op(x, lax.ppermute(x, axis, xor_pairs(n, d)))
    return x


def reduce_scatter(x, axis, n):
    idx = lax.axis_index(axis)
    nb = n.bit_length() - 1
    chunk = x.shape[0] // n
    rest = x.shape[1:]
    x = x.reshape((2,) * nb + (chunk,) + rest)
    left = list(range(nb))
    for d in bits_of(n):
        t = left.index(nb - 1 - (d.bit_length() - 1))
        bit = (idx // d) % 2
        keep = lax.dynamic_index_in_dim(x, bit, axis=t, keepdims=False)
        send = lax.dynamic_index_in_dim(x, 1 - bit, axis=t, keepdims=False)
        x = keep + lax.ppermute(send, axis, xor_pairs(n, d))
        left.pop(t)
    return x.reshape((chunk,) + rest)


def all_gather(x, axis, n, flat=True):
    idx = lax.axis_index(axis)
    nb = n.bit_length() - 1
    have = []
    for d in reversed(bits_of(n)):
        pos = nb - 1 - (d.bit_length() - 1)
        t = sum(1 for h in have if h < pos)
        other = lax.ppermute(x, axis, xor_pairs(n, d))
        bit = (idx // d) % 2
        x = jnp.where(bit == 0, jnp.stack([x, other], axis=t), jnp.stack([other, x], axis=t))
        have.append(pos)
        have.sort()
    x = x.reshape((n,) + x.shape[nb:])
    if flat:
        x = x.reshape((-1,) + x.shape[2:])
    return x


def make_local(n_group, n_inner):
    def local(flow_field, sketch_rows, sketch_cols, sketch_depth, bit_widths, bin_edges):
        rows_i, cols_j, depth_k = flow_field.shape
        rank = sketch_depth.shape[1]
        n1 = rows_i * n_inner
        n2 = cols_j * n_group
        k_blk = depth_k // n_group
        r_blk = rank // n_inner
        s_blk = rank // n_group
        g = lax.axis_index("group")
        p = lax.axis_index("inner")

        reduced = jnp.einsum("ijk,kr->ijr", flow_field, sketch_depth, precision=precise)
        mode_one = jnp.einsum("ijr,jr->ir", reduced, sketch_cols, precision=precise)
        mode_two = jnp.einsum("ijr,ir->jr", reduced, sketch_rows, precision=precise)
        mode_two = all_reduce(mode_two, "inner", n_inner)
        mode_one = all_reduce(mode_one, "group", n_group)
        eye = jnp.eye(rank, dtype=jnp.float32)
        lower_two = jnp.linalg.cholesky(all_reduce(gram_of(mode_two), "group", n_group))
        basis_two = jax.scipy.linalg.solve_triangular(lower_two, mode_two.T, lower=True).T
        inverse_two = jax.scipy.linalg.solve_triangular(lower_two, eye, lower=True)
        lower_one = jnp.linalg.cholesky(all_reduce(gram_of(mode_one), "inner", n_inner))
        basis_one = jax.scipy.linalg.solve_triangular(lower_one, mode_one.T, lower=True).T
        inverse_one = jax.scipy.linalg.solve_triangular(lower_one, eye, lower=True)
        basis_two_all = all_gather(basis_two, "group", n_group)

        along_two = jnp.einsum("ijk,js->kis", flow_field, mode_two, precision=precise)
        along_two = reduce_scatter(along_two, "group", n_group)
        partial = jnp.einsum("kis,ir->krs", along_two, mode_one, precision=precise)
        partial = partial.reshape(k_blk * rank, rank)
        core_part = reduce_scatter(partial, "inner", n_inner)
        raw_k = all_gather(core_part, "inner", n_inner).reshape(k_blk, rank, rank)
        core_k = jnp.einsum("qr,krt->kqt", inverse_one, raw_k, precision=precise)
        core_k = jnp.einsum("krt,st->krs", core_k, inverse_two, precision=precise)
        peak = jnp.max(jnp.abs(core_k))

        core_rows = lax.dynamic_slice_in_dim(core_k, p * r_blk, r_blk, axis=1)
        mark = jnp.broadcast_to(peak, (1, r_blk, rank))
        gathered = all_gather(jnp.concatenate([core_rows, mark], axis=0), "group", n_group, flat=False)
        core_rows = gathered[:, :k_blk].reshape(depth_k, r_blk, rank)
        peak = jnp.max(gathered[:, k_blk:])
        core_block = lax.dynamic_slice_in_dim(core_rows, g * s_blk, s_blk, axis=2)
        core_block = jnp.transpose(core_block, (1, 2, 0))

        levels = jnp.exp2(bit_widths.astype(jnp.float32) - 1.0) - 1.0
        step = peak / levels
        residual_k = soft_residual(core_k, step)
        residual_block = soft_residual(core_block, step)

        error_scale = error_boost * math.sqrt(n1 * n2) / rank
        edge_values = bin_edges.astype(jnp.float32)
        mixed = jnp.einsum("ir,bkrs->sbik", basis_one, residual_k, precision=lax.Precision.HIGH)
        nb = mixed.shape[1]
        mixed = mixed.reshape(rank, nb * rows_i * k_blk)
        field_error = error_scale * jnp.dot(basis_two_all, mixed, precision=lax.Precision.HIGH)
        energy_part = (jnp.sum(field_error * field_error, axis=0) / n2).reshape(nb, rows_i, k_blk)
        shifted = field_error + 0.5
        ramp_part = jnp.stack(
            [
                (
                    jnp.sum(
                        jnp.clip(shifted, edge_values[index_edge], edge_values[index_edge] + 1.0),
                        axis=0,
                    )
                    - field_error.shape[0] * edge_values[index_edge]
                ).reshape(nb, rows_i, k_blk).sum(axis=2)
                for index_edge in range(NEDGE)
            ],
            axis=-1,
        )
        energy_slot = jnp.zeros((nb, rows_i, depth_k), jnp.float32)
        energy_slot = lax.dynamic_update_slice_in_dim(energy_slot, energy_part, g * k_blk, axis=2)
        packed = all_reduce(jnp.concatenate([energy_slot, ramp_part], axis=2), "group", n_group)
        energy = packed[:, :, :depth_k]
        ramp_sums = packed[:, :, depth_k:]
        histogram = (ramp_sums[..., :-1] - ramp_sums[..., 1:]) * (NBINS / (n2 * depth_k))
        return (basis_one, basis_two, core_block, residual_block, energy, histogram)

    return local


def solution(mesh):
    in_specs = (P("inner", "group", None), P("inner", None), P("group", None), P(), P(), P())
    out_specs = (
        P("inner", None),
        P("group", None),
        P("inner", "group", None),
        P(None, "inner", "group", None),
        P(None, "inner", None),
        P(None, "inner", None),
    )
    local = make_local(mesh.shape["group"], mesh.shape["inner"])
    return jax.shard_map(local, mesh=mesh, in_specs=in_specs, out_specs=out_specs, check_vma=False)
```

```python
import math

import jax
import jax.numpy as jnp
from jax import lax
from jax.sharding import PartitionSpec as P

NEDGE = 9
NBINS = 8


precise = lax.Precision.HIGHEST
two_pi = 2.0 * 3.141592653589793
error_boost = 16.0


def gram_of(sketch):
    return jnp.dot(sketch.T, sketch, precision=precise)


def orthonormal_rows(sketch, gram_matrix):
    lower_factor = jnp.linalg.cholesky(gram_matrix)
    return jax.scipy.linalg.solve_triangular(lower_factor, sketch.T, lower=True).T


def soft_residual(core_values, step_size):
    shape = (-1,) + (1,) * core_values.ndim
    return -jnp.sin(two_pi * core_values[None] / step_size.reshape(shape)) / two_pi


def xor_pairs(n, d):
    return [(a, a ^ d) for a in range(n)]


def bits_of(n):
    return [1 << t for t in range(n.bit_length() - 1)]


def all_reduce(x, axis, n, op=jnp.add):
    for d in bits_of(n):
        x = op(x, lax.ppermute(x, axis, xor_pairs(n, d)))
    return x


def reduce_scatter(x, axis, n):
    idx = lax.axis_index(axis)
    nb = n.bit_length() - 1
    chunk = x.shape[0] // n
    rest = x.shape[1:]
    x = x.reshape((2,) * nb + (chunk,) + rest)
    left = list(range(nb))
    for d in bits_of(n):
        t = left.index(nb - 1 - (d.bit_length() - 1))
        bit = (idx // d) % 2
        keep = lax.dynamic_index_in_dim(x, bit, axis=t, keepdims=False)
        send = lax.dynamic_index_in_dim(x, 1 - bit, axis=t, keepdims=False)
        x = keep + lax.ppermute(send, axis, xor_pairs(n, d))
        left.pop(t)
    return x.reshape((chunk,) + rest)


def all_gather(x, axis, n, flat=True):
    idx = lax.axis_index(axis)
    nb = n.bit_length() - 1
    have = []
    for d in reversed(bits_of(n)):
        pos = nb - 1 - (d.bit_length() - 1)
        t = sum(1 for h in have if h < pos)
        other = lax.ppermute(x, axis, xor_pairs(n, d))
        bit = (idx // d) % 2
        x = jnp.where(bit == 0, jnp.stack([x, other], axis=t), jnp.stack([other, x], axis=t))
        have.append(pos)
        have.sort()
    x = x.reshape((n,) + x.shape[nb:])
    if flat:
        x = x.reshape((-1,) + x.shape[2:])
    return x


def make_local(n_group, n_inner):
    def local(flow_field, sketch_rows, sketch_cols, sketch_depth, bit_widths, bin_edges):
        rows_i, cols_j, depth_k = flow_field.shape
        rank = sketch_depth.shape[1]
        n1 = rows_i * n_inner
        n2 = cols_j * n_group
        k_blk = depth_k // n_group
        r_blk = rank // n_inner
        s_blk = rank // n_group
        g = lax.axis_index("group")
        p = lax.axis_index("inner")

        reduced = jnp.einsum("ijk,kr->ijr", flow_field, sketch_depth, precision=precise)
        mode_one = jnp.einsum("ijr,jr->ir", reduced, sketch_cols, precision=precise)
        mode_two = jnp.einsum("ijr,ir->jr", reduced, sketch_rows, precision=precise)
        mode_two = all_reduce(mode_two, "inner", n_inner)
        mode_one = all_reduce(mode_one, "group", n_group)
        gram_two = all_reduce(gram_of(mode_two), "group", n_group)
        gram_one = all_reduce(gram_of(mode_one), "inner", n_inner)
        lower = jnp.linalg.cholesky(jnp.stack([gram_one, gram_two]))
        eye = jnp.broadcast_to(jnp.eye(rank, dtype=jnp.float32), lower.shape)
        inverse = jax.scipy.linalg.solve_triangular(lower, eye, lower=True)
        inverse_one = inverse[0]
        inverse_two = inverse[1]
        basis_one = jnp.dot(mode_one, inverse_one.T, precision=precise)
        basis_two = jnp.dot(mode_two, inverse_two.T, precision=precise)
        basis_two_all = all_gather(basis_two, "group", n_group)

        along_two = jnp.einsum("ijk,js->kis", flow_field, mode_two, precision=precise)
        along_two = reduce_scatter(along_two, "group", n_group)
        partial = jnp.einsum("kis,ir->krs", along_two, mode_one, precision=precise)
        partial = partial.reshape(k_blk * rank, rank)
        core_part = reduce_scatter(partial, "inner", n_inner)
        raw_k = all_gather(core_part, "inner", n_inner).reshape(k_blk, rank, rank)
        core_k = jnp.einsum("qr,krt->kqt", inverse_one, raw_k, precision=precise)
        core_k = jnp.einsum("krt,st->krs", core_k, inverse_two, precision=precise)
        peak = jnp.max(jnp.abs(core_k))

        core_rows = lax.dynamic_slice_in_dim(core_k, p * r_blk, r_blk, axis=1)
        mark = jnp.broadcast_to(peak, (1, r_blk, rank))
        gathered = all_gather(jnp.concatenate([core_rows, mark], axis=0), "group", n_group, flat=False)
        core_rows = gathered[:, :k_blk].reshape(depth_k, r_blk, rank)
        peak = jnp.max(gathered[:, k_blk:])
        core_block = lax.dynamic_slice_in_dim(core_rows, g * s_blk, s_blk, axis=2)
        core_block = jnp.transpose(core_block, (1, 2, 0))

        levels = jnp.exp2(bit_widths.astype(jnp.float32) - 1.0) - 1.0
        step = peak / levels
        residual_k = soft_residual(core_k, step)
        residual_block = soft_residual(core_block, step)

        error_scale = error_boost * math.sqrt(n1 * n2) / rank
        edge_values = bin_edges.astype(jnp.float32)
        mixed = jnp.einsum("ir,bkrs->sbik", basis_one, residual_k, precision=lax.Precision.HIGH)
        nb = mixed.shape[1]
        mixed = mixed.reshape(rank, nb * rows_i * k_blk)
        field_error = error_scale * jnp.dot(basis_two_all, mixed, precision=lax.Precision.HIGH)
        energy_part = (jnp.sum(field_error * field_error, axis=0) / n2).reshape(nb, rows_i, k_blk)
        shifted = field_error + 0.5
        ramp_part = jnp.stack(
            [
                (
                    jnp.sum(
                        jnp.clip(shifted, edge_values[index_edge], edge_values[index_edge] + 1.0),
                        axis=0,
                    )
                    - field_error.shape[0] * edge_values[index_edge]
                ).reshape(nb, rows_i, k_blk).sum(axis=2)
                for index_edge in range(NEDGE)
            ],
            axis=-1,
        )
        energy_slot = jnp.zeros((nb, rows_i, depth_k), jnp.float32)
        energy_slot = lax.dynamic_update_slice_in_dim(energy_slot, energy_part, g * k_blk, axis=2)
        packed = all_reduce(jnp.concatenate([energy_slot, ramp_part], axis=2), "group", n_group)
        energy = packed[:, :, :depth_k]
        ramp_sums = packed[:, :, depth_k:]
        histogram = (ramp_sums[..., :-1] - ramp_sums[..., 1:]) * (NBINS / (n2 * depth_k))
        return (basis_one, basis_two, core_block, residual_block, energy, histogram)

    return local


def solution(mesh):
    in_specs = (P("inner", "group", None), P("inner", None), P("group", None), P(), P(), P())
    out_specs = (
        P("inner", None),
        P("group", None),
        P("inner", "group", None),
        P(None, "inner", "group", None),
        P(None, "inner", None),
        P(None, "inner", None),
    )
    local = make_local(mesh.shape["group"], mesh.shape["inner"])
    return jax.shard_map(local, mesh=mesh, in_specs=in_specs, out_specs=out_specs, check_vma=False)
```

```python
import math

import jax
import jax.numpy as jnp
from jax import lax
from jax.sharding import PartitionSpec as P

NEDGE = 9
NBINS = 8


precise = lax.Precision.HIGHEST
two_pi = 2.0 * 3.141592653589793
error_boost = 16.0


def gram_of(sketch):
    return jnp.dot(sketch.T, sketch, precision=precise)


def orthonormal_rows(sketch, gram_matrix):
    lower_factor = jnp.linalg.cholesky(gram_matrix)
    return jax.scipy.linalg.solve_triangular(lower_factor, sketch.T, lower=True).T


def soft_residual(core_values, step_size):
    shape = (-1,) + (1,) * core_values.ndim
    return -jnp.sin(two_pi * core_values[None] / step_size.reshape(shape)) / two_pi


def xor_pairs(n, d):
    return [(a, a ^ d) for a in range(n)]


def bits_of(n):
    return [1 << t for t in range(n.bit_length() - 1)]


def all_reduce(x, axis, n, op=jnp.add):
    for d in bits_of(n):
        x = op(x, lax.ppermute(x, axis, xor_pairs(n, d)))
    return x


def reduce_scatter(x, axis, n, extras=()):
    idx = lax.axis_index(axis)
    nb = n.bit_length() - 1
    chunk = x.shape[0] // n
    rest = x.shape[1:]
    x = x.reshape((2,) * nb + (chunk,) + rest)
    extras = list(extras)
    left = list(range(nb))
    for d in bits_of(n):
        t = left.index(nb - 1 - (d.bit_length() - 1))
        bit = (idx // d) % 2
        keep = lax.dynamic_index_in_dim(x, bit, axis=t, keepdims=False)
        send = lax.dynamic_index_in_dim(x, 1 - bit, axis=t, keepdims=False)
        flat = send.reshape(-1, send.shape[-1])
        got = lax.ppermute(jnp.concatenate([flat] + extras, axis=0), axis, xor_pairs(n, d))
        x = keep + got[: flat.shape[0]].reshape(send.shape)
        at = flat.shape[0]
        for e in range(len(extras)):
            size = extras[e].shape[0]
            extras[e] = extras[e] + got[at : at + size]
            at += size
        left.pop(t)
    x = x.reshape((chunk,) + rest)
    return (x, extras) if extras else x


def all_gather(x, axis, n, flat=True):
    idx = lax.axis_index(axis)
    nb = n.bit_length() - 1
    have = []
    for d in reversed(bits_of(n)):
        pos = nb - 1 - (d.bit_length() - 1)
        t = sum(1 for h in have if h < pos)
        other = lax.ppermute(x, axis, xor_pairs(n, d))
        bit = (idx // d) % 2
        x = jnp.where(bit == 0, jnp.stack([x, other], axis=t), jnp.stack([other, x], axis=t))
        have.append(pos)
        have.sort()
    x = x.reshape((n,) + x.shape[nb:])
    if flat:
        x = x.reshape((-1,) + x.shape[2:])
    return x


def make_local(n_group, n_inner):
    def local(flow_field, sketch_rows, sketch_cols, sketch_depth, bit_widths, bin_edges):
        rows_i, cols_j, depth_k = flow_field.shape
        rank = sketch_depth.shape[1]
        n1 = rows_i * n_inner
        n2 = cols_j * n_group
        k_blk = depth_k // n_group
        r_blk = rank // n_inner
        s_blk = rank // n_group
        g = lax.axis_index("group")
        p = lax.axis_index("inner")

        reduced = jnp.einsum("ijk,kr->ijr", flow_field, sketch_depth, precision=precise)
        mode_one = jnp.einsum("ijr,jr->ir", reduced, sketch_cols, precision=precise)
        mode_two = jnp.einsum("ijr,ir->jr", reduced, sketch_rows, precision=precise)
        mode_two = all_reduce(mode_two, "inner", n_inner)
        along_two = jnp.einsum("ijk,js->kis", flow_field, mode_two, precision=precise)
        along_two, (mode_one, gram_two) = reduce_scatter(
            along_two, "group", n_group, extras=(mode_one, gram_of(mode_two))
        )
        partial = jnp.einsum("kis,ir->krs", along_two, mode_one, precision=precise)
        partial = partial.reshape(k_blk * rank, rank)
        core_part, (gram_one,) = reduce_scatter(partial, "inner", n_inner, extras=(gram_of(mode_one),))
        lower = jnp.linalg.cholesky(jnp.stack([gram_one, gram_two]))
        eye = jnp.broadcast_to(jnp.eye(rank, dtype=jnp.float32), lower.shape)
        inverse = jax.scipy.linalg.solve_triangular(lower, eye, lower=True)
        inverse_one = inverse[0]
        inverse_two = inverse[1]
        basis_one = jnp.dot(mode_one, inverse_one.T, precision=precise)
        basis_two = jnp.dot(mode_two, inverse_two.T, precision=precise)
        basis_two_all = all_gather(basis_two, "group", n_group)
        raw_k = all_gather(core_part, "inner", n_inner).reshape(k_blk, rank, rank)
        core_k = jnp.einsum("qr,krt->kqt", inverse_one, raw_k, precision=precise)
        core_k = jnp.einsum("krt,st->krs", core_k, inverse_two, precision=precise)
        peak = jnp.max(jnp.abs(core_k))

        core_rows = lax.dynamic_slice_in_dim(core_k, p * r_blk, r_blk, axis=1)
        mark = jnp.broadcast_to(peak, (1, r_blk, rank))
        gathered = all_gather(jnp.concatenate([core_rows, mark], axis=0), "group", n_group, flat=False)
        core_rows = gathered[:, :k_blk].reshape(depth_k, r_blk, rank)
        peak = jnp.max(gathered[:, k_blk:])
        core_block = lax.dynamic_slice_in_dim(core_rows, g * s_blk, s_blk, axis=2)
        core_block = jnp.transpose(core_block, (1, 2, 0))

        levels = jnp.exp2(bit_widths.astype(jnp.float32) - 1.0) - 1.0
        step = peak / levels
        residual_k = soft_residual(core_k, step)
        residual_block = soft_residual(core_block, step)

        error_scale = error_boost * math.sqrt(n1 * n2) / rank
        edge_values = bin_edges.astype(jnp.float32)
        mixed = jnp.einsum("ir,bkrs->sbik", basis_one, residual_k, precision=lax.Precision.HIGH)
        nb = mixed.shape[1]
        mixed = mixed.reshape(rank, nb * rows_i * k_blk)
        field_error = error_scale * jnp.dot(basis_two_all, mixed, precision=lax.Precision.HIGH)
        energy_part = (jnp.sum(field_error * field_error, axis=0) / n2).reshape(nb, rows_i, k_blk)
        shifted = field_error + 0.5
        ramp_part = jnp.stack(
            [
                (
                    jnp.sum(
                        jnp.clip(shifted, edge_values[index_edge], edge_values[index_edge] + 1.0),
                        axis=0,
                    )
                    - field_error.shape[0] * edge_values[index_edge]
                ).reshape(nb, rows_i, k_blk).sum(axis=2)
                for index_edge in range(NEDGE)
            ],
            axis=-1,
        )
        energy_slot = jnp.zeros((nb, rows_i, depth_k), jnp.float32)
        energy_slot = lax.dynamic_update_slice_in_dim(energy_slot, energy_part, g * k_blk, axis=2)
        packed = all_reduce(jnp.concatenate([energy_slot, ramp_part], axis=2), "group", n_group)
        energy = packed[:, :, :depth_k]
        ramp_sums = packed[:, :, depth_k:]
        histogram = (ramp_sums[..., :-1] - ramp_sums[..., 1:]) * (NBINS / (n2 * depth_k))
        return (basis_one, basis_two, core_block, residual_block, energy, histogram)

    return local


def solution(mesh):
    in_specs = (P("inner", "group", None), P("inner", None), P("group", None), P(), P(), P())
    out_specs = (
        P("inner", None),
        P("group", None),
        P("inner", "group", None),
        P(None, "inner", "group", None),
        P(None, "inner", None),
        P(None, "inner", None),
    )
    local = make_local(mesh.shape["group"], mesh.shape["inner"])
    return jax.shard_map(local, mesh=mesh, in_specs=in_specs, out_specs=out_specs, check_vma=False)
```

```python
import math

import jax
import jax.numpy as jnp
from jax import lax
from jax.sharding import PartitionSpec as P

NEDGE = 9
NBINS = 8


precise = lax.Precision.HIGHEST
two_pi = 2.0 * 3.141592653589793
error_boost = 16.0


def gram_of(sketch):
    return jnp.dot(sketch.T, sketch, precision=precise)


def orthonormal_rows(sketch, gram_matrix):
    lower_factor = jnp.linalg.cholesky(gram_matrix)
    return jax.scipy.linalg.solve_triangular(lower_factor, sketch.T, lower=True).T


def soft_residual(core_values, step_size):
    shape = (-1,) + (1,) * core_values.ndim
    return -jnp.sin(two_pi * core_values[None] / step_size.reshape(shape)) / two_pi


def xor_pairs(n, d):
    return [(a, a ^ d) for a in range(n)]


def bits_of(n):
    return [1 << t for t in range(n.bit_length() - 1)]


def all_reduce(x, axis, n, op=jnp.add):
    for d in bits_of(n):
        x = op(x, lax.ppermute(x, axis, xor_pairs(n, d)))
    return x


def reduce_scatter(x, axis, n):
    idx = lax.axis_index(axis)
    nb = n.bit_length() - 1
    chunk = x.shape[0] // n
    rest = x.shape[1:]
    x = x.reshape((2,) * nb + (chunk,) + rest)
    left = list(range(nb))
    for d in bits_of(n):
        t = left.index(nb - 1 - (d.bit_length() - 1))
        bit = (idx // d) % 2
        keep = lax.dynamic_index_in_dim(x, bit, axis=t, keepdims=False)
        send = lax.dynamic_index_in_dim(x, 1 - bit, axis=t, keepdims=False)
        x = keep + lax.ppermute(send, axis, xor_pairs(n, d))
        left.pop(t)
    return x.reshape((chunk,) + rest)


def all_gather(x, axis, n, flat=True):
    idx = lax.axis_index(axis)
    nb = n.bit_length() - 1
    have = []
    for d in reversed(bits_of(n)):
        pos = nb - 1 - (d.bit_length() - 1)
        t = sum(1 for h in have if h < pos)
        other = lax.ppermute(x, axis, xor_pairs(n, d))
        bit = (idx // d) % 2
        x = jnp.where(bit == 0, jnp.stack([x, other], axis=t), jnp.stack([other, x], axis=t))
        have.append(pos)
        have.sort()
    x = x.reshape((n,) + x.shape[nb:])
    if flat:
        x = x.reshape((-1,) + x.shape[2:])
    return x


def make_local(n_group, n_inner):
    def local(flow_field, sketch_rows, sketch_cols, sketch_depth, bit_widths, bin_edges):
        rows_i, cols_j, depth_k = flow_field.shape
        rank = sketch_depth.shape[1]
        n1 = rows_i * n_inner
        n2 = cols_j * n_group
        k_blk = depth_k // n_group
        r_blk = rank // n_inner
        s_blk = rank // n_group
        g = lax.axis_index("group")
        p = lax.axis_index("inner")

        reduced = jnp.einsum("ijk,kr->ijr", flow_field, sketch_depth, precision=precise)
        mode_one = jnp.einsum("ijr,jr->ir", reduced, sketch_cols, precision=precise)
        mode_two = jnp.einsum("ijr,ir->jr", reduced, sketch_rows, precision=precise)
        mode_two = all_reduce(mode_two, "inner", n_inner)
        mode_one = all_reduce(mode_one, "group", n_group)
        eye = jnp.eye(rank, dtype=jnp.float32)
        mode_two_all = all_gather(mode_two, "group", n_group)
        lower_two = jnp.linalg.cholesky(gram_of(mode_two_all))
        basis_two_all = jax.scipy.linalg.solve_triangular(lower_two, mode_two_all.T, lower=True).T
        basis_two = lax.dynamic_slice_in_dim(basis_two_all, g * cols_j, cols_j, axis=0)
        inverse_two = jax.scipy.linalg.solve_triangular(lower_two, eye, lower=True)
        lower_one = jnp.linalg.cholesky(all_reduce(gram_of(mode_one), "inner", n_inner))
        basis_one = jax.scipy.linalg.solve_triangular(lower_one, mode_one.T, lower=True).T
        inverse_one = jax.scipy.linalg.solve_triangular(lower_one, eye, lower=True)

        along_two = jnp.einsum("ijk,js->kis", flow_field, mode_two, precision=precise)
        along_two = reduce_scatter(along_two, "group", n_group)
        partial = jnp.einsum("kis,ir->krs", along_two, mode_one, precision=precise)
        partial = partial.reshape(k_blk * rank, rank)
        core_part = reduce_scatter(partial, "inner", n_inner)
        raw_k = all_gather(core_part, "inner", n_inner).reshape(k_blk, rank, rank)
        core_k = jnp.einsum("qr,krt->kqt", inverse_one, raw_k, precision=precise)
        core_k = jnp.einsum("krt,st->krs", core_k, inverse_two, precision=precise)
        peak = jnp.max(jnp.abs(core_k))

        core_rows = lax.dynamic_slice_in_dim(core_k, p * r_blk, r_blk, axis=1)
        mark = jnp.broadcast_to(peak, (1, r_blk, rank))
        gathered = all_gather(jnp.concatenate([core_rows, mark], axis=0), "group", n_group, flat=False)
        core_rows = gathered[:, :k_blk].reshape(depth_k, r_blk, rank)
        peak = jnp.max(gathered[:, k_blk:])
        core_block = lax.dynamic_slice_in_dim(core_rows, g * s_blk, s_blk, axis=2)
        core_block = jnp.transpose(core_block, (1, 2, 0))

        levels = jnp.exp2(bit_widths.astype(jnp.float32) - 1.0) - 1.0
        step = peak / levels
        residual_k = soft_residual(core_k, step)
        residual_block = soft_residual(core_block, step)

        error_scale = error_boost * math.sqrt(n1 * n2) / rank
        edge_values = bin_edges.astype(jnp.float32)
        mixed = jnp.einsum("ir,bkrs->sbik", basis_one, residual_k, precision=lax.Precision.HIGH)
        nb = mixed.shape[1]
        mixed = mixed.reshape(rank, nb * rows_i * k_blk)
        field_error = error_scale * jnp.dot(basis_two_all, mixed, precision=lax.Precision.HIGH)
        energy_part = (jnp.sum(field_error * field_error, axis=0) / n2).reshape(nb, rows_i, k_blk)
        shifted = field_error + 0.5
        ramp_part = jnp.stack(
            [
                (
                    jnp.sum(
                        jnp.clip(shifted, edge_values[index_edge], edge_values[index_edge] + 1.0),
                        axis=0,
                    )
                    - field_error.shape[0] * edge_values[index_edge]
                ).reshape(nb, rows_i, k_blk).sum(axis=2)
                for index_edge in range(NEDGE)
            ],
            axis=-1,
        )
        energy_slot = jnp.zeros((nb, rows_i, depth_k), jnp.float32)
        energy_slot = lax.dynamic_update_slice_in_dim(energy_slot, energy_part, g * k_blk, axis=2)
        packed = all_reduce(jnp.concatenate([energy_slot, ramp_part], axis=2), "group", n_group)
        energy = packed[:, :, :depth_k]
        ramp_sums = packed[:, :, depth_k:]
        histogram = (ramp_sums[..., :-1] - ramp_sums[..., 1:]) * (NBINS / (n2 * depth_k))
        return (basis_one, basis_two, core_block, residual_block, energy, histogram)

    return local


def solution(mesh):
    in_specs = (P("inner", "group", None), P("inner", None), P("group", None), P(), P(), P())
    out_specs = (
        P("inner", None),
        P("group", None),
        P("inner", "group", None),
        P(None, "inner", "group", None),
        P(None, "inner", None),
        P(None, "inner", None),
    )
    local = make_local(mesh.shape["group"], mesh.shape["inner"])
    return jax.shard_map(local, mesh=mesh, in_specs=in_specs, out_specs=out_specs, check_vma=False)
```

```python
import math

import jax
import jax.numpy as jnp
from jax import lax
from jax.sharding import PartitionSpec as P

NEDGE = 9
NBINS = 8


precise = lax.Precision.HIGHEST
two_pi = 2.0 * 3.141592653589793
error_boost = 16.0


def gram_of(sketch):
    return jnp.dot(sketch.T, sketch, precision=precise)


def orthonormal_rows(sketch, gram_matrix):
    lower_factor = jnp.linalg.cholesky(gram_matrix)
    return jax.scipy.linalg.solve_triangular(lower_factor, sketch.T, lower=True).T


def soft_residual(core_values, step_size):
    shape = (-1,) + (1,) * core_values.ndim
    return -jnp.sin(two_pi * core_values[None] / step_size.reshape(shape)) / two_pi


def xor_pairs(n, d):
    return [(a, a ^ d) for a in range(n)]


def bits_of(n):
    return [1 << t for t in range(n.bit_length() - 1)]


def all_reduce(x, axis, n, op=jnp.add):
    for d in bits_of(n):
        x = op(x, lax.ppermute(x, axis, xor_pairs(n, d)))
    return x


def reduce_scatter(x, axis, n):
    idx = lax.axis_index(axis)
    nb = n.bit_length() - 1
    chunk = x.shape[0] // n
    rest = x.shape[1:]
    x = x.reshape((2,) * nb + (chunk,) + rest)
    left = list(range(nb))
    for d in bits_of(n):
        t = left.index(nb - 1 - (d.bit_length() - 1))
        bit = (idx // d) % 2
        keep = lax.dynamic_index_in_dim(x, bit, axis=t, keepdims=False)
        send = lax.dynamic_index_in_dim(x, 1 - bit, axis=t, keepdims=False)
        x = keep + lax.ppermute(send, axis, xor_pairs(n, d))
        left.pop(t)
    return x.reshape((chunk,) + rest)


def all_gather(x, axis, n, flat=True):
    idx = lax.axis_index(axis)
    nb = n.bit_length() - 1
    have = []
    for d in reversed(bits_of(n)):
        pos = nb - 1 - (d.bit_length() - 1)
        t = sum(1 for h in have if h < pos)
        other = lax.ppermute(x, axis, xor_pairs(n, d))
        bit = (idx // d) % 2
        x = jnp.where(bit == 0, jnp.stack([x, other], axis=t), jnp.stack([other, x], axis=t))
        have.append(pos)
        have.sort()
    x = x.reshape((n,) + x.shape[nb:])
    if flat:
        x = x.reshape((-1,) + x.shape[2:])
    return x


def make_local(n_group, n_inner):
    def local(flow_field, sketch_rows, sketch_cols, sketch_depth, bit_widths, bin_edges):
        rows_i, cols_j, depth_k = flow_field.shape
        rank = sketch_depth.shape[1]
        n1 = rows_i * n_inner
        n2 = cols_j * n_group
        k_blk = depth_k // n_group
        r_blk = rank // n_inner
        s_blk = rank // n_group
        g = lax.axis_index("group")
        p = lax.axis_index("inner")

        reduced = jnp.einsum("ijk,kr->ijr", flow_field, sketch_depth, precision=precise)
        mode_one = jnp.einsum("ijr,jr->ir", reduced, sketch_cols, precision=precise)
        mode_two = jnp.einsum("ijr,ir->jr", reduced, sketch_rows, precision=precise)
        mode_one = all_reduce(mode_one, "group", n_group)
        packed = all_reduce(jnp.concatenate([gram_of(mode_one), mode_two], axis=0), "inner", n_inner)
        gram_one = packed[:rank]
        mode_two = packed[rank:]
        eye = jnp.eye(rank, dtype=jnp.float32)
        lower_two = jnp.linalg.cholesky(all_reduce(gram_of(mode_two), "group", n_group))
        basis_two = jax.scipy.linalg.solve_triangular(lower_two, mode_two.T, lower=True).T
        inverse_two = jax.scipy.linalg.solve_triangular(lower_two, eye, lower=True)
        lower_one = jnp.linalg.cholesky(gram_one)
        basis_one = jax.scipy.linalg.solve_triangular(lower_one, mode_one.T, lower=True).T
        inverse_one = jax.scipy.linalg.solve_triangular(lower_one, eye, lower=True)
        basis_two_all = all_gather(basis_two, "group", n_group)

        along_two = jnp.einsum("ijk,js->kis", flow_field, mode_two, precision=precise)
        along_two = reduce_scatter(along_two, "group", n_group)
        partial = jnp.einsum("kis,ir->krs", along_two, mode_one, precision=precise)
        partial = partial.reshape(k_blk * rank, rank)
        core_part = reduce_scatter(partial, "inner", n_inner)
        raw_k = all_gather(core_part, "inner", n_inner).reshape(k_blk, rank, rank)
        core_k = jnp.einsum("qr,krt->kqt", inverse_one, raw_k, precision=precise)
        core_k = jnp.einsum("krt,st->krs", core_k, inverse_two, precision=precise)
        peak = jnp.max(jnp.abs(core_k))

        core_rows = lax.dynamic_slice_in_dim(core_k, p * r_blk, r_blk, axis=1)
        mark = jnp.broadcast_to(peak, (1, r_blk, rank))
        gathered = all_gather(jnp.concatenate([core_rows, mark], axis=0), "group", n_group, flat=False)
        core_rows = gathered[:, :k_blk].reshape(depth_k, r_blk, rank)
        peak = jnp.max(gathered[:, k_blk:])
        core_block = lax.dynamic_slice_in_dim(core_rows, g * s_blk, s_blk, axis=2)
        core_block = jnp.transpose(core_block, (1, 2, 0))

        levels = jnp.exp2(bit_widths.astype(jnp.float32) - 1.0) - 1.0
        step = peak / levels
        residual_k = soft_residual(core_k, step)
        residual_block = soft_residual(core_block, step)

        error_scale = error_boost * math.sqrt(n1 * n2) / rank
        edge_values = bin_edges.astype(jnp.float32)
        mixed = jnp.einsum("ir,bkrs->sbik", basis_one, residual_k, precision=lax.Precision.HIGH)
        nb = mixed.shape[1]
        mixed = mixed.reshape(rank, nb * rows_i * k_blk)
        field_error = error_scale * jnp.dot(basis_two_all, mixed, precision=lax.Precision.HIGH)
        energy_part = (jnp.sum(field_error * field_error, axis=0) / n2).reshape(nb, rows_i, k_blk)
        shifted = field_error + 0.5
        ramp_part = jnp.stack(
            [
                (
                    jnp.sum(
                        jnp.clip(shifted, edge_values[index_edge], edge_values[index_edge] + 1.0),
                        axis=0,
                    )
                    - field_error.shape[0] * edge_values[index_edge]
                ).reshape(nb, rows_i, k_blk).sum(axis=2)
                for index_edge in range(NEDGE)
            ],
            axis=-1,
        )
        energy_slot = jnp.zeros((nb, rows_i, depth_k), jnp.float32)
        energy_slot = lax.dynamic_update_slice_in_dim(energy_slot, energy_part, g * k_blk, axis=2)
        packed = all_reduce(jnp.concatenate([energy_slot, ramp_part], axis=2), "group", n_group)
        energy = packed[:, :, :depth_k]
        ramp_sums = packed[:, :, depth_k:]
        histogram = (ramp_sums[..., :-1] - ramp_sums[..., 1:]) * (NBINS / (n2 * depth_k))
        return (basis_one, basis_two, core_block, residual_block, energy, histogram)

    return local


def solution(mesh):
    in_specs = (P("inner", "group", None), P("inner", None), P("group", None), P(), P(), P())
    out_specs = (
        P("inner", None),
        P("group", None),
        P("inner", "group", None),
        P(None, "inner", "group", None),
        P(None, "inner", None),
        P(None, "inner", None),
    )
    local = make_local(mesh.shape["group"], mesh.shape["inner"])
    return jax.shard_map(local, mesh=mesh, in_specs=in_specs, out_specs=out_specs, check_vma=False)
```
